512 devices in a mesh: node: 64 (over z, x), local: 8 (over y, core).
Axes of the slice: x: 4, y: 4, z: 16, core: 2. Of those that a mesh axis runs over, the one named last changes fastest.
Arguments:
- grad_out: bfloat16 [8192, 7168], P('node', 'local'), may hold values from -6 to 6
- probs: bfloat16 [8192, 8], P('node'), may hold values from 0.099609375 to 2.5
- node_list: int32 [8192, 4], P('node'), may hold values from 0 to 63, all different within a row; in each aligned block of 128 rows (0 to 127, 128 to 255, ...) at most 12 rows name the same one
- weight_down: bfloat16 [128, 1024, 7168], P('node', 'local'), may hold values from -0.1875 to 0.1875
- saved_hidden: bfloat16 [128, 768, 1024], P('node', None, 'local'), may hold values from -0.1875 to 0.1875
Outputs:
- grad_hidden: bfloat16 [128, 768, 1024], P('node', None, 'local')
- grad_probs: float32 [8192, 8], P('node')
The draws below stay inside these ranges and needn't reach their ends.
Inputs may be any that keep to these rules, and one draw needn't show every extreme that they name: `node_list`: each token lists 4 different nodes. Among the 128 tokens of one index of node, at most 12 list any one node, and some node is listed by exactly 12 of them.
All inputs are finite; a program needn't handle non-finite values.
Results may differ from the reference program's by a relative error of at most 0.001.
Values may be sent and summed in bfloat16 or wider, within the bound.
No kernel may reach another device: no remote copies, remote signals or barrier semaphores. Data moves between devices by JAX's collectives and lax.ppermute only.
A program may use at most 128 MiB of HBM per device.

```python
import math
import jax
import jax.numpy as jnp
import numpy as np
from jax import lax

D = 7168
FF = 1024
EXP_NODE = 2
MAXNODE = 4
TOPK = 8
TOK_NODE = 128
CAP = 12
TOKENS = 8192
EXPERTS = 128
N_NODE = 64


def block_levels(stream_key, dims, cuts, least, high):
    loudness, own = 1.0, jax.random.fold_in(stream_key, 6)
    for position, parts in cuts:
        steps = jnp.exp(jax.random.uniform(jax.random.fold_in(own, position), (parts,), jnp.float32, least / len(cuts), high / len(cuts)))
        loudness = loudness * jnp.repeat(steps, dims[position] // parts).reshape([-1 if axis == position else 1 for axis in range(len(dims))])
    return loudness


def deal_out(own_key, own, number, rows, number_of, top, limit, skew):
    order = jax.random.permutation(own_key, number_of)
    crowded, ordinary = portions_of(number_of, rows * top, limit, skew, True), portions_of(number_of, rows * top, limit, skew, False)
    places = jnp.arange(number_of)

    def named(sizes, offset_by):
        used = int((sizes > 0).sum())
        fixed = max(1, used // 4)
        moved = fixed + (places - fixed + offset_by * (used - fixed)) % max(1, number_of - fixed)
        return jnp.zeros((number_of,), jnp.int32).at[order[jnp.where(places < fixed, places, moved)]].set(jnp.asarray(sizes, jnp.int32))

    sizes = jnp.where(number % 4 == 0, named(crowded, number // 4), named(ordinary, number - number // 4 - 1))
    mixed = jax.random.permutation(jax.random.fold_in(own, 3), number_of)
    donor, receiver = mixed[0:number_of // 2 * 2:2], mixed[1:number_of // 2 * 2:2]
    margin = jnp.minimum(sizes[donor] - 1, limit - sizes[receiver]) // 2
    margin = jnp.where((donor == order[0]) | (receiver == order[0]) | (sizes[receiver] == 0), 0, jnp.maximum(margin, 0))
    moved = jax.random.randint(jax.random.fold_in(own, 4), (number_of // 2,), 0, 1 << 20) % (margin + 1)
    sizes = sizes.at[donor].add(-moved).at[receiver].add(moved)
    members = jnp.searchsorted(jnp.cumsum(sizes), jnp.arange(rows * top), side="right").astype(jnp.int32)
    listing = members.reshape(top, rows).T
    listing = listing[jax.random.permutation(jax.random.fold_in(own, 1), rows)]
    offset_by = jax.random.randint(jax.random.fold_in(own, 2), (rows, 1), 0, top)
    return jnp.take_along_axis(listing, (jnp.arange(top)[None, :] + offset_by) % top, axis=1)


def portions_of(count, total, bound, skew, full):
    loads = [(1 << 20) // math.isqrt(grade ** skew) + 1 for grade in range(1, count + 1)]
    largest = bound if full else min(bound, max(-(-total // count), total * loads[0] // sum(loads)))
    least = 1 if total - largest >= count - 1 else 0
    given, surplus = [largest] + [least] * (count - 1), total - largest - least * (count - 1)
    while surplus > 0:
        movable = [i for i in range(1, count) if given[i] < largest] or [i for i in range(1, count) if given[i] < bound]
        mass, remaining = sum([loads[i] for i in movable]), surplus
        for i in movable:
            addition = min(bound - given[i], max(1, remaining * loads[i] // mass), surplus)
            given[i] = given[i] + addition
            surplus = surplus - addition
    return np.array(given)


def normal_values(rng, dims, width, limit, split=(), held_as=jnp.bfloat16):
    loudness = block_levels(rng, dims, split, -0.22, 0.18) if split else 1.0
    entries = jax.random.normal(rng, dims, jnp.float32) * width * loudness
    return jnp.minimum(jnp.maximum(entries, -limit), limit).astype(held_as)


def setup_inputs(seed: int = 0) -> dict:
    splits = jax.random.split(jax.random.key(seed), 6)
    grad_out = normal_values(splits[0], (TOKENS, D), 1.0, 6.0, ((0, 64), (1, 8)))
    probs = jnp.clip(jnp.exp(math.log(2.5) - 3.2227897 * jax.random.uniform(splits[1], (TOKENS, TOPK), jnp.float32) ** block_levels(splits[1], (TOKENS, TOPK), ((0, 64),), -0.2, 0.2)), 0.099609375, 2.5).astype(jnp.bfloat16)
    node_list_keys = jax.random.split(jax.random.fold_in(splits[2], 1), TOKENS // TOK_NODE)
    node_list_turns = jax.random.permutation(jax.random.fold_in(splits[2], 3), TOKENS // TOK_NODE)
    node_list = jax.vmap(lambda own, number: deal_out(jax.random.fold_in(splits[2], 2), own, number, TOK_NODE, N_NODE, MAXNODE, CAP, 2))(node_list_keys, node_list_turns).reshape((TOKENS, MAXNODE))
    weight_down = normal_values(splits[3], (EXPERTS, FF, D), FF ** -0.5, 0.1875, ((0, 64), (1, 8)))
    saved_hidden = normal_values(splits[4], (EXPERTS, N_NODE * CAP, FF), 0.03, 0.1875, ((0, 64), (2, 8)))
    return {"grad_out": grad_out, "probs": probs, "node_list": node_list, "weight_down": weight_down, "saved_hidden": saved_hidden}


def reference(grad_out, probs, node_list, weight_down, saved_hidden):
    listed = node_list.reshape(N_NODE, TOK_NODE, MAXNODE)
    node_ids = jnp.arange(N_NODE, dtype=jnp.int32)
    member = jnp.sum((listed[..., None] == node_ids).astype(jnp.int32), axis=2)
    arrival = jnp.cumsum(member, axis=1) - member
    slot_pos = jnp.take_along_axis(arrival, listed, axis=2).astype(jnp.int32)
    source_ids = jnp.broadcast_to(jnp.arange(N_NODE, dtype=jnp.int32)[:, None, None], listed.shape)
    token_ids = source_ids * TOK_NODE + jnp.arange(TOK_NODE, dtype=jnp.int32)[None, :, None]
    choice_ids = jnp.broadcast_to(jnp.arange(MAXNODE, dtype=jnp.int32)[None, None, :], listed.shape)
    table_token = jnp.full((N_NODE, N_NODE, CAP), TOKENS, jnp.int32).at[listed, source_ids, slot_pos].set(token_ids)
    table_choice = jnp.zeros((N_NODE, N_NODE, CAP), jnp.int32).at[listed, source_ids, slot_pos].set(choice_ids)

    def one_expert(expert):
        home = expert // EXP_NODE
        which = expert % EXP_NODE
        tokens_here = table_token[home].reshape(-1)
        valid = tokens_here < TOKENS
        safe_index = jnp.minimum(tokens_here, TOKENS - 1)
        rows = jnp.where(valid[:, None], grad_out[safe_index], jnp.zeros((), grad_out.dtype))
        grads = jnp.dot(rows, weight_down[expert].T, preferred_element_type=jnp.float32)
        column = (EXP_NODE * table_choice[home].reshape(-1) + which).astype(jnp.int32)
        weights = jnp.where(valid, probs[safe_index, column].astype(jnp.float32), jnp.zeros((), jnp.float32))
        hidden = (weights[:, None] * grads).astype(jnp.bfloat16)
        scores = jnp.sum(saved_hidden[expert].astype(jnp.float32) * grads, axis=1)
        return hidden, scores, column

    grad_hidden, scores, columns = lax.map(one_expert, jnp.arange(EXPERTS, dtype=jnp.int32))
    token_index = jnp.repeat(table_token.reshape(N_NODE, -1), EXP_NODE, axis=0)
    grad_probs = jnp.zeros((TOKENS, TOPK), jnp.float32).at[token_index, columns].set(scores, mode="drop")
    return grad_hidden, grad_probs
```

```python
import jax
import jax.numpy as jnp
from jax import lax
from jax.sharding import PartitionSpec as P


def gather_slots(source, source_row, slot_valid):
    padded = jnp.concatenate([source, jnp.zeros((1, source.shape[1]), source.dtype)], axis=0)
    index = jnp.where(slot_valid, source_row, source.shape[0])
    return jnp.take(padded, index, axis=0)


def on_device(grad_out, probs, node_list, weight_down, saved_hidden):
    node_count = lax.axis_size("node")
    tok_rows = node_list.shape[0]
    route_count = node_list.shape[1]
    slot_rows = saved_hidden.shape[1]
    capacity = slot_rows // node_count
    expert_count = weight_down.shape[0]
    node_ids = lax.broadcasted_iota(jnp.int32, (tok_rows, route_count, node_count), 2)
    listed = (node_list[:, :, None] == node_ids).astype(jnp.float32)
    member = jnp.sum((node_list[:, :, None] == node_ids).astype(jnp.int32), axis=1)
    arrival = jnp.cumsum(member, axis=0) - member
    positions = lax.broadcasted_iota(jnp.int32, (tok_rows, node_count, capacity), 2)
    select_mask = (arrival[:, :, None] == positions) & (member[:, :, None] == 1)
    select_count = select_mask.astype(jnp.int32)
    token_iota = lax.broadcasted_iota(jnp.int32, (tok_rows, node_count, capacity), 0)
    source_row = jnp.sum(select_count * token_iota, axis=0)
    slot_valid = jnp.sum(select_count, axis=0) > 0
    select_full = select_mask.astype(jnp.float32)
    grouped = probs.reshape(tok_rows, route_count, expert_count).astype(jnp.float32)
    picked = jnp.einsum("tjm,tjc->tmc", listed, grouped, precision=lax.Precision.HIGHEST)
    prob_send = jnp.einsum(
        "tms,tmc->msc", select_full, picked, precision=lax.Precision.HIGHEST
    ).astype(jnp.bfloat16)
    rows_send = gather_slots(grad_out, source_row, slot_valid)
    width = grad_out.shape[1]
    payload = jnp.concatenate(
        [
            rows_send.reshape(node_count, capacity * width),
            prob_send.reshape(node_count, capacity * expert_count),
        ],
        axis=1,
    )
    payload_in = lax.all_to_all(payload, "node", split_axis=0, concat_axis=0, tiled=True)
    rows_in = payload_in[:, : capacity * width].reshape(slot_rows, width)
    prob_in = payload_in[:, capacity * width :]
    full_rows = lax.all_gather(rows_in, "local", axis=0, tiled=False)
    local_count = full_rows.shape[0]
    weight_split = weight_down.reshape(
        expert_count, weight_down.shape[1], local_count, width
    )
    hidden_grads = jnp.einsum(
        "lrd,ehld->erh",
        full_rows,
        weight_split,
        preferred_element_type=jnp.float32,
    )
    scales = jnp.transpose(prob_in.reshape(slot_rows, expert_count).astype(jnp.float32))
    grad_hidden = (scales[:, :, None] * hidden_grads).astype(jnp.bfloat16)
    partial_value = jnp.sum(saved_hidden.astype(jnp.float32) * hidden_grads, axis=2)
    partial_value = jnp.transpose(partial_value).reshape(node_count, capacity, expert_count)
    summed = lax.psum(partial_value, "local")
    returned = lax.all_to_all(summed, "node", split_axis=0, concat_axis=0, tiled=True)
    per_node = jnp.einsum("tms,msc->tmc", select_full, returned, precision=lax.Precision.HIGHEST)
    grad_probs = jnp.einsum("tjm,tmc->tjc", listed, per_node, precision=lax.Precision.HIGHEST)
    return (grad_hidden, grad_probs.reshape(tok_rows, route_count * expert_count))


def solution(mesh):
    return jax.shard_map(
        on_device,
        mesh=mesh,
        in_specs=(
            P("node", "local"),
            P("node", None),
            P("node", None),
            P("node", "local", None),
            P("node", None, "local"),
        ),
        out_specs=(P("node", None, "local"), P("node", None)),
        check_vma=False,
    )
```

```python
import jax
import jax.numpy as jnp
from jax import lax
from jax.sharding import PartitionSpec as P


def gather_slots(source, source_row, slot_valid):
    padded = jnp.concatenate([source, jnp.zeros((1, source.shape[1]), source.dtype)], axis=0)
    index = jnp.where(slot_valid, source_row, source.shape[0])
    return jnp.take(padded, index, axis=0)


def on_device(grad_out, probs, node_list, weight_down, saved_hidden):
    node_count = lax.axis_size("node")
    tok_rows = node_list.shape[0]
    route_count = node_list.shape[1]
    slot_rows = saved_hidden.shape[1]
    capacity = slot_rows // node_count
    expert_count = weight_down.shape[0]
    node_ids = lax.broadcasted_iota(jnp.int32, (tok_rows, route_count, node_count), 2)
    listed = (node_list[:, :, None] == node_ids).astype(jnp.float32)
    member = jnp.sum((node_list[:, :, None] == node_ids).astype(jnp.int32), axis=1)
    arrival = jnp.cumsum(member, axis=0) - member
    positions = lax.broadcasted_iota(jnp.int32, (tok_rows, node_count, capacity), 2)
    select_mask = (arrival[:, :, None] == positions) & (member[:, :, None] == 1)
    select_count = select_mask.astype(jnp.int32)
    token_iota = lax.broadcasted_iota(jnp.int32, (tok_rows, node_count, capacity), 0)
    source_row = jnp.sum(select_count * token_iota, axis=0)
    slot_valid = jnp.sum(select_count, axis=0) > 0
    select_full = select_mask.astype(jnp.float32)
    grouped = probs.reshape(tok_rows, route_count, expert_count).astype(jnp.float32)
    picked = jnp.einsum("tjm,tjc->tmc", listed, grouped, precision=lax.Precision.HIGHEST)
    prob_send = jnp.einsum(
        "tms,tmc->msc", select_full, picked, precision=lax.Precision.HIGHEST
    ).astype(jnp.bfloat16)
    rows_send = gather_slots(grad_out, source_row, slot_valid)
    width = grad_out.shape[1]
    payload = jnp.concatenate(
        [
            rows_send.reshape(node_count, capacity * width),
            prob_send.reshape(node_count, capacity * expert_count),
        ],
        axis=1,
    )
    payload_in = lax.all_to_all(payload, "node", split_axis=0, concat_axis=0, tiled=True)
    rows_in = payload_in[:, : capacity * width].reshape(slot_rows, width)
    prob_in = payload_in[:, capacity * width :]
    full_rows = lax.all_gather(rows_in, "local", axis=0, tiled=False)
    local_count = full_rows.shape[0]
    weight_split = weight_down.reshape(
        expert_count, weight_down.shape[1], local_count, width
    )
    hidden_grads = jnp.einsum(
        "lrd,ehld->erh",
        full_rows,
        weight_split,
        preferred_element_type=jnp.float32,
    )
    scales = jnp.transpose(prob_in.reshape(slot_rows, expert_count).astype(jnp.float32))
    grad_hidden = (scales[:, :, None] * hidden_grads).astype(jnp.bfloat16)
    partial_value = jnp.sum(saved_hidden.astype(jnp.float32) * hidden_grads, axis=2)
    partial_value = jnp.transpose(partial_value).reshape(node_count, capacity, expert_count)
    local_count = lax.axis_size("local")
    gathered = lax.all_gather(partial_value, ("node", "local"), axis=0, tiled=False)
    gathered = gathered.reshape(node_count, local_count, node_count, capacity, expert_count)
    mine = lax.dynamic_index_in_dim(gathered, lax.axis_index("node"), axis=2, keepdims=False)
    returned = jnp.sum(mine, axis=1)
    per_node = jnp.einsum("tms,msc->tmc", select_full, returned, precision=lax.Precision.HIGHEST)
    grad_probs = jnp.einsum("tjm,tmc->tjc", listed, per_node, precision=lax.Precision.HIGHEST)
    return (grad_hidden, grad_probs.reshape(tok_rows, route_count * expert_count))


def solution(mesh):
    return jax.shard_map(
        on_device,
        mesh=mesh,
        in_specs=(
            P("node", "local"),
            P("node", None),
            P("node", None),
            P("node", "local", None),
            P("node", None, "local"),
        ),
        out_specs=(P("node", None, "local"), P("node", None)),
        check_vma=False,
    )
```

```python
import jax
import jax.numpy as jnp
from jax import lax
from jax.sharding import PartitionSpec as P


def gather_slots(source, source_row, slot_valid):
    padded = jnp.concatenate([source, jnp.zeros((1, source.shape[1]), source.dtype)], axis=0)
    index = jnp.where(slot_valid, source_row, source.shape[0])
    return jnp.take(padded, index, axis=0)


def on_device(grad_out, probs, node_list, weight_down, saved_hidden):
    node_count = lax.axis_size("node")
    tok_rows = node_list.shape[0]
    route_count = node_list.shape[1]
    slot_rows = saved_hidden.shape[1]
    capacity = slot_rows // node_count
    expert_count = weight_down.shape[0]
    node_ids = lax.broadcasted_iota(jnp.int32, (tok_rows, route_count, node_count), 2)
    listed = (node_list[:, :, None] == node_ids).astype(jnp.float32)
    member = jnp.sum((node_list[:, :, None] == node_ids).astype(jnp.int32), axis=1)
    arrival = jnp.cumsum(member, axis=0) - member
    positions = lax.broadcasted_iota(jnp.int32, (tok_rows, node_count, capacity), 2)
    select_mask = (arrival[:, :, None] == positions) & (member[:, :, None] == 1)
    select_count = select_mask.astype(jnp.int32)
    token_iota = lax.broadcasted_iota(jnp.int32, (tok_rows, node_count, capacity), 0)
    source_row = jnp.sum(select_count * token_iota, axis=0)
    slot_valid = jnp.sum(select_count, axis=0) > 0
    select_full = select_mask.astype(jnp.float32)
    grouped = probs.reshape(tok_rows, route_count, expert_count).astype(jnp.float32)
    picked = jnp.einsum("tjm,tjc->tmc", listed, grouped, precision=lax.Precision.HIGHEST)
    prob_send = jnp.einsum(
        "tms,tmc->msc", select_full, picked, precision=lax.Precision.HIGHEST
    ).astype(jnp.bfloat16)
    rows_send = gather_slots(grad_out, source_row, slot_valid)
    width = grad_out.shape[1]
    payload = jnp.concatenate(
        [
            rows_send.reshape(node_count, capacity * width),
            prob_send.reshape(node_count, capacity * expert_count),
        ],
        axis=1,
    )
    payload_in = lax.all_to_all(payload, "node", split_axis=0, concat_axis=0, tiled=True)
    rows_in = payload_in[:, : capacity * width].reshape(slot_rows, width)
    prob_in = payload_in[:, capacity * width :]
    full_rows = lax.all_gather(rows_in, "local", axis=0, tiled=False)
    local_count = full_rows.shape[0]
    weight_split = weight_down.reshape(
        expert_count, weight_down.shape[1], local_count, width
    )
    hidden_grads = jnp.einsum(
        "lrd,ehld->erh",
        full_rows,
        weight_split,
        preferred_element_type=jnp.float32,
    )
    scales = jnp.transpose(prob_in.reshape(slot_rows, expert_count).astype(jnp.float32))
    grad_hidden = (scales[:, :, None] * hidden_grads).astype(jnp.bfloat16)
    partial_value = jnp.sum(saved_hidden.astype(jnp.float32) * hidden_grads, axis=2)
    partial_value = jnp.transpose(partial_value).reshape(node_count, capacity, expert_count)
    summed = jnp.sum(lax.all_gather(partial_value, "local", axis=0, tiled=False), axis=0)
    returned = lax.all_to_all(summed, "node", split_axis=0, concat_axis=0, tiled=True)
    per_node = jnp.einsum("tms,msc->tmc", select_full, returned, precision=lax.Precision.HIGHEST)
    grad_probs = jnp.einsum("tjm,tmc->tjc", listed, per_node, precision=lax.Precision.HIGHEST)
    return (grad_hidden, grad_probs.reshape(tok_rows, route_count * expert_count))


def solution(mesh):
    return jax.shard_map(
        on_device,
        mesh=mesh,
        in_specs=(
            P("node", "local"),
            P("node", None),
            P("node", None),
            P("node", "local", None),
            P("node", None, "local"),
        ),
        out_specs=(P("node", None, "local"), P("node", None)),
        check_vma=False,
    )
```

```python
import jax
import jax.numpy as jnp
from jax import lax
from jax.sharding import PartitionSpec as P


def gather_slots(source, source_row, slot_valid):
    padded = jnp.concatenate([source, jnp.zeros((1, source.shape[1]), source.dtype)], axis=0)
    index = jnp.where(slot_valid, source_row, source.shape[0])
    return jnp.take(padded, index, axis=0)


def on_device(grad_out, probs, node_list, weight_down, saved_hidden):
    node_count = lax.axis_size("node")
    tok_rows = node_list.shape[0]
    route_count = node_list.shape[1]
    slot_rows = saved_hidden.shape[1]
    capacity = slot_rows // node_count
    expert_count = weight_down.shape[0]
    node_ids = lax.broadcasted_iota(jnp.int32, (tok_rows, route_count, node_count), 2)
    listed = (node_list[:, :, None] == node_ids).astype(jnp.float32)
    member = jnp.sum((node_list[:, :, None] == node_ids).astype(jnp.int32), axis=1)
    arrival = jnp.cumsum(member, axis=0) - member
    positions = lax.broadcasted_iota(jnp.int32, (tok_rows, node_count, capacity), 2)
    select_mask = (arrival[:, :, None] == positions) & (member[:, :, None] == 1)
    select_count = select_mask.astype(jnp.int32)
    token_iota = lax.broadcasted_iota(jnp.int32, (tok_rows, node_count, capacity), 0)
    source_row = jnp.sum(select_count * token_iota, axis=0)
    slot_valid = jnp.sum(select_count, axis=0) > 0
    select_full = select_mask.astype(jnp.float32)
    grouped = probs.reshape(tok_rows, route_count, expert_count).astype(jnp.float32)
    picked = jnp.einsum("tjm,tjc->tmc", listed, grouped, precision=lax.Precision.HIGHEST)
    prob_send = jnp.einsum(
        "tms,tmc->msc", select_full, picked, precision=lax.Precision.HIGHEST
    ).astype(jnp.bfloat16)
    rows_send = gather_slots(grad_out, source_row, slot_valid)
    width = grad_out.shape[1]
    payload = jnp.concatenate(
        [
            rows_send.reshape(node_count, capacity * width),
            prob_send.reshape(node_count, capacity * expert_count),
        ],
        axis=1,
    )
    payload_in = lax.all_to_all(payload, "node", split_axis=0, concat_axis=0, tiled=True)
    rows_in = payload_in[:, : capacity * width].reshape(slot_rows, width)
    prob_in = payload_in[:, capacity * width :]
    local_count = lax.axis_size("local")
    hidden_local = weight_down.shape[1]
    weight_split = weight_down.reshape(expert_count, hidden_local, local_count, width)
    weight_cols = lax.all_to_all(weight_split, "local", split_axis=2, concat_axis=1, tiled=True)
    weight_cols = weight_cols.reshape(expert_count, hidden_local * local_count, width)
    partial_grads = jnp.einsum(
        "rd,ehd->erh",
        rows_in,
        weight_cols,
        preferred_element_type=jnp.float32,
    )
    hidden_grads = lax.psum_scatter(partial_grads, "local", scatter_dimension=2, tiled=True)
    scales = jnp.transpose(prob_in.reshape(slot_rows, expert_count).astype(jnp.float32))
    grad_hidden = (scales[:, :, None] * hidden_grads).astype(jnp.bfloat16)
    partial_value = jnp.sum(saved_hidden.astype(jnp.float32) * hidden_grads, axis=2)
    partial_value = jnp.transpose(partial_value).reshape(node_count, capacity, expert_count)
    summed = jnp.sum(lax.all_gather(partial_value, "local", axis=0, tiled=False), axis=0)
    returned = lax.all_to_all(summed, "node", split_axis=0, concat_axis=0, tiled=True)
    per_node = jnp.einsum("tms,msc->tmc", select_full, returned, precision=lax.Precision.HIGHEST)
    grad_probs = jnp.einsum("tjm,tmc->tjc", listed, per_node, precision=lax.Precision.HIGHEST)
    return (grad_hidden, grad_probs.reshape(tok_rows, route_count * expert_count))


def solution(mesh):
    return jax.shard_map(
        on_device,
        mesh=mesh,
        in_specs=(
            P("node", "local"),
            P("node", None),
            P("node", None),
            P("node", "local", None),
            P("node", None, "local"),
        ),
        out_specs=(P("node", None, "local"), P("node", None)),
        check_vma=False,
    )
```

```python
import jax
import jax.numpy as jnp
from jax import lax
from jax.sharding import PartitionSpec as P


def gather_slots(source, source_row, slot_valid):
    padded = jnp.concatenate([source, jnp.zeros((1, source.shape[1]), source.dtype)], axis=0)
    index = jnp.where(slot_valid, source_row, source.shape[0])
    return jnp.take(padded, index, axis=0)


def on_device(grad_out, probs, node_list, weight_down, saved_hidden):
    node_count = lax.axis_size("node")
    tok_rows = node_list.shape[0]
    route_count = node_list.shape[1]
    slot_rows = saved_hidden.shape[1]
    capacity = slot_rows // node_count
    expert_count = weight_down.shape[0]
    node_ids = lax.broadcasted_iota(jnp.int32, (tok_rows, route_count, node_count), 2)
    listed = (node_list[:, :, None] == node_ids).astype(jnp.float32)
    member = jnp.sum((node_list[:, :, None] == node_ids).astype(jnp.int32), axis=1)
    arrival = jnp.cumsum(member, axis=0) - member
    positions = lax.broadcasted_iota(jnp.int32, (tok_rows, node_count, capacity), 2)
    select_mask = (arrival[:, :, None] == positions) & (member[:, :, None] == 1)
    select_count = select_mask.astype(jnp.int32)
    token_iota = lax.broadcasted_iota(jnp.int32, (tok_rows, node_count, capacity), 0)
    source_row = jnp.sum(select_count * token_iota, axis=0)
    slot_valid = jnp.sum(select_count, axis=0) > 0
    select_full = select_mask.astype(jnp.float32)
    grouped = probs.reshape(tok_rows, route_count, expert_count).astype(jnp.float32)
    picked = jnp.einsum("tjm,tjc->tmc", listed, grouped, precision=lax.Precision.HIGHEST)
    prob_send = jnp.einsum(
        "tms,tmc->msc", select_full, picked, precision=lax.Precision.HIGHEST
    ).astype(jnp.bfloat16)
    rows_send = gather_slots(grad_out, source_row, slot_valid)
    width = grad_out.shape[1]
    payload = jnp.concatenate(
        [
            rows_send.reshape(node_count, capacity * width),
            prob_send.reshape(node_count, capacity * expert_count),
        ],
        axis=1,
    )
    payload_in = lax.all_to_all(payload, "node", split_axis=0, concat_axis=0, tiled=True)
    rows_in = payload_in[:, : capacity * width].reshape(slot_rows, width)
    prob_in = payload_in[:, capacity * width :]
    local_count = lax.axis_size("local")
    local_index = lax.axis_index("local")
    pieces = []
    for step in range(local_count):
        target = (local_index + step) % local_count
        piece = lax.dynamic_slice_in_dim(weight_down, target * width, width, axis=2)
        if step:
            pairs = [(j, (j + step) % local_count) for j in range(local_count)]
            piece = lax.ppermute(piece, "local", perm=pairs)
        pieces.append(piece)
    stacked = jnp.stack(pieces, axis=0)
    block_order = (local_index - jnp.arange(local_count, dtype=jnp.int32)) % local_count
    weight_blocks = jnp.take(stacked, block_order, axis=0)
    partial_grads = jnp.einsum(
        "rd,behd->erbh",
        rows_in,
        weight_blocks,
        preferred_element_type=jnp.float32,
    ).reshape(expert_count, slot_rows, -1)
    hidden_grads = lax.psum_scatter(partial_grads, "local", scatter_dimension=2, tiled=True)
    scales = jnp.transpose(prob_in.reshape(slot_rows, expert_count).astype(jnp.float32))
    grad_hidden = (scales[:, :, None] * hidden_grads).astype(jnp.bfloat16)
    partial_value = jnp.sum(saved_hidden.astype(jnp.float32) * hidden_grads, axis=2)
    partial_value = jnp.transpose(partial_value).reshape(node_count, capacity, expert_count)
    summed = jnp.sum(lax.all_gather(partial_value, "local", axis=0, tiled=False), axis=0)
    returned = lax.all_to_all(summed, "node", split_axis=0, concat_axis=0, tiled=True)
    per_node = jnp.einsum("tms,msc->tmc", select_full, returned, precision=lax.Precision.HIGHEST)
    grad_probs = jnp.einsum("tjm,tmc->tjc", listed, per_node, precision=lax.Precision.HIGHEST)
    return (grad_hidden, grad_probs.reshape(tok_rows, route_count * expert_count))


def solution(mesh):
    return jax.shard_map(
        on_device,
        mesh=mesh,
        in_specs=(
            P("node", "local"),
            P("node", None),
            P("node", None),
            P("node", "local", None),
            P("node", None, "local"),
        ),
        out_specs=(P("node", None, "local"), P("node", None)),
        check_vma=False,
    )
```

```python
import jax
import jax.numpy as jnp
from jax import lax
from jax.sharding import PartitionSpec as P


def gather_slots(source, source_row, slot_valid):
    padded = jnp.concatenate([source, jnp.zeros((1, source.shape[1]), source.dtype)], axis=0)
    index = jnp.where(slot_valid, source_row, source.shape[0])
    return jnp.take(padded, index, axis=0)


def on_device(grad_out, probs, node_list, weight_down, saved_hidden):
    node_count = lax.axis_size("node")
    tok_rows = node_list.shape[0]
    route_count = node_list.shape[1]
    slot_rows = saved_hidden.shape[1]
    capacity = slot_rows // node_count
    expert_count = weight_down.shape[0]
    node_ids = lax.broadcasted_iota(jnp.int32, (tok_rows, route_count, node_count), 2)
    listed = (node_list[:, :, None] == node_ids).astype(jnp.float32)
    member = jnp.sum((node_list[:, :, None] == node_ids).astype(jnp.int32), axis=1)
    arrival = jnp.cumsum(member, axis=0) - member
    positions = lax.broadcasted_iota(jnp.int32, (tok_rows, node_count, capacity), 2)
    select_mask = (arrival[:, :, None] == positions) & (member[:, :, None] == 1)
    select_count = select_mask.astype(jnp.int32)
    token_iota = lax.broadcasted_iota(jnp.int32, (tok_rows, node_count, capacity), 0)
    source_row = jnp.sum(select_count * token_iota, axis=0)
    slot_valid = jnp.sum(select_count, axis=0) > 0
    select_full = select_mask.astype(jnp.float32)
    grouped = probs.reshape(tok_rows, route_count, expert_count).astype(jnp.float32)
    picked = jnp.einsum("tjm,tjc->tmc", listed, grouped, precision=lax.Precision.HIGHEST)
    prob_send = jnp.einsum(
        "tms,tmc->msc", select_full, picked, precision=lax.Precision.HIGHEST
    ).astype(jnp.bfloat16)
    rows_send = gather_slots(grad_out, source_row, slot_valid)
    width = grad_out.shape[1]
    payload = jnp.concatenate(
        [
            rows_send.reshape(node_count, capacity * width),
            prob_send.reshape(node_count, capacity * expert_count),
        ],
        axis=1,
    )
    payload_in = lax.all_to_all(payload, "node", split_axis=0, concat_axis=0, tiled=True)
    rows_in = payload_in[:, : capacity * width].reshape(slot_rows, width)
    prob_in = payload_in[:, capacity * width :]
    local_count = lax.axis_size("local")
    local_index = lax.axis_index("local")
    pieces = []
    for step in range(local_count):
        target = (local_index + step) % local_count
        piece = lax.dynamic_slice_in_dim(weight_down, target * width, width, axis=2)
        if step:
            pairs = [(j, (j + step) % local_count) for j in range(local_count)]
            piece = lax.ppermute(piece, "local", perm=pairs)
        pieces.append(piece)
    stacked = jnp.stack(pieces, axis=0)
    block_order = (local_index - jnp.arange(local_count, dtype=jnp.int32)) % local_count
    weight_blocks = jnp.take(stacked, block_order, axis=0)
    partial_grads = jnp.einsum(
        "rd,behd->berh",
        rows_in,
        weight_blocks,
        preferred_element_type=jnp.float32,
    )
    saved_blocks = lax.all_gather(saved_hidden, "local", axis=0, tiled=False)
    partial_scores = jnp.sum(saved_blocks.astype(jnp.float32) * partial_grads, axis=(0, 3))
    lane = partial_grads.shape[3]
    score_rows = -(-slot_rows // lane)
    extra_rows = -(-score_rows // 8) * 8
    score_block = jnp.pad(
        partial_scores, ((0, 0), (0, extra_rows * lane - slot_rows))
    ).reshape(expert_count, extra_rows, lane)
    extended = jnp.concatenate(
        [partial_grads, jnp.broadcast_to(score_block[None], (local_count,) + score_block.shape)],
        axis=2,
    )
    reduced = lax.psum_scatter(extended, "local", scatter_dimension=0, tiled=True)[0]
    hidden_grads = reduced[:, :slot_rows, :]
    scores = reduced[:, slot_rows:, :].reshape(expert_count, -1)[:, :slot_rows]
    scales = jnp.transpose(prob_in.reshape(slot_rows, expert_count).astype(jnp.float32))
    grad_hidden = (scales[:, :, None] * hidden_grads).astype(jnp.bfloat16)
    summed = jnp.transpose(scores).reshape(node_count, capacity, expert_count)
    returned = lax.all_to_all(summed, "node", split_axis=0, concat_axis=0, tiled=True)
    per_node = jnp.einsum("tms,msc->tmc", select_full, returned, precision=lax.Precision.HIGHEST)
    grad_probs = jnp.einsum("tjm,tmc->tjc", listed, per_node, precision=lax.Precision.HIGHEST)
    return (grad_hidden, grad_probs.reshape(tok_rows, route_count * expert_count))


def solution(mesh):
    return jax.shard_map(
        on_device,
        mesh=mesh,
        in_specs=(
            P("node", "local"),
            P("node", None),
            P("node", None),
            P("node", "local", None),
            P("node", None, "local"),
        ),
        out_specs=(P("node", None, "local"), P("node", None)),
        check_vma=False,
    )
```

```python
import jax
import jax.numpy as jnp
from jax import lax
from jax.sharding import PartitionSpec as P


def gather_slots(source, source_row, slot_valid):
    padded = jnp.concatenate([source, jnp.zeros((1, source.shape[1]), source.dtype)], axis=0)
    index = jnp.where(slot_valid, source_row, source.shape[0])
    return jnp.take(padded, index, axis=0)


def on_device(grad_out, probs, node_list, weight_down, saved_hidden):
    node_count = lax.axis_size("node")
    tok_rows = node_list.shape[0]
    route_count = node_list.shape[1]
    slot_rows = saved_hidden.shape[1]
    capacity = slot_rows // node_count
    expert_count = weight_down.shape[0]
    node_ids = lax.broadcasted_iota(jnp.int32, (tok_rows, route_count, node_count), 2)
    listed = (node_list[:, :, None] == node_ids).astype(jnp.float32)
    member = jnp.sum((node_list[:, :, None] == node_ids).astype(jnp.int32), axis=1)
    arrival = jnp.cumsum(member, axis=0) - member
    positions = lax.broadcasted_iota(jnp.int32, (tok_rows, node_count, capacity), 2)
    select_mask = (arrival[:, :, None] == positions) & (member[:, :, None] == 1)
    select_count = select_mask.astype(jnp.int32)
    token_iota = lax.broadcasted_iota(jnp.int32, (tok_rows, node_count, capacity), 0)
    source_row = jnp.sum(select_count * token_iota, axis=0)
    slot_valid = jnp.sum(select_count, axis=0) > 0
    select_full = select_mask.astype(jnp.float32)
    grouped = probs.reshape(tok_rows, route_count, expert_count).astype(jnp.float32)
    picked = jnp.einsum("tjm,tjc->tmc", listed, grouped, precision=lax.Precision.HIGHEST)
    prob_send = jnp.einsum(
        "tms,tmc->msc", select_full, picked, precision=lax.Precision.HIGHEST
    ).astype(jnp.bfloat16)
    rows_send = gather_slots(grad_out, source_row, slot_valid)
    width = grad_out.shape[1]
    payload = jnp.concatenate(
        [
            rows_send.reshape(node_count, capacity * width),
            prob_send.reshape(node_count, capacity * expert_count),
        ],
        axis=1,
    )
    payload_in = lax.all_to_all(payload, "node", split_axis=0, concat_axis=0, tiled=True)
    rows_in = payload_in[:, : capacity * width].reshape(slot_rows, width)
    prob_in = payload_in[:, capacity * width :]
    local_count = lax.axis_size("local")
    local_index = lax.axis_index("local")
    pieces = []
    for step in range(local_count):
        target = (local_index + step) % local_count
        piece = lax.dynamic_slice_in_dim(weight_down, target * width, width, axis=2)
        if step:
            pairs = [(j, (j + step) % local_count) for j in range(local_count)]
            piece = lax.ppermute(piece, "local", perm=pairs)
        pieces.append(piece)
    stacked = jnp.stack(pieces, axis=0)
    block_order = (local_index - jnp.arange(local_count, dtype=jnp.int32)) % local_count
    weight_blocks = jnp.take(stacked, block_order, axis=0)
    partial_grads = jnp.einsum(
        "rd,behd->erbh",
        rows_in,
        weight_blocks,
        preferred_element_type=jnp.float32,
    ).reshape(expert_count, slot_rows, -1)
    saved_blocks = lax.all_gather(saved_hidden, "local", axis=0, tiled=False)
    partial_scores = jnp.einsum(
        "berh,erbh->er",
        saved_blocks.astype(jnp.float32),
        partial_grads.reshape(expert_count, slot_rows, local_count, -1),
        precision=lax.Precision.HIGHEST,
    )
    partial_value = jnp.transpose(partial_scores).reshape(node_count, capacity, expert_count)
    summed = jnp.sum(lax.all_gather(partial_value, "local", axis=0, tiled=False), axis=0)
    hidden_grads = lax.psum_scatter(partial_grads, "local", scatter_dimension=2, tiled=True)
    scales = jnp.transpose(prob_in.reshape(slot_rows, expert_count).astype(jnp.float32))
    grad_hidden = (scales[:, :, None] * hidden_grads).astype(jnp.bfloat16)
    returned = lax.all_to_all(summed, "node", split_axis=0, concat_axis=0, tiled=True)
    per_node = jnp.einsum("tms,msc->tmc", select_full, returned, precision=lax.Precision.HIGHEST)
    grad_probs = jnp.einsum("tjm,tmc->tjc", listed, per_node, precision=lax.Precision.HIGHEST)
    return (grad_hidden, grad_probs.reshape(tok_rows, route_count * expert_count))


def solution(mesh):
    return jax.shard_map(
        on_device,
        mesh=mesh,
        in_specs=(
            P("node", "local"),
            P("node", None),
            P("node", None),
            P("node", "local", None),
            P("node", None, "local"),
        ),
        out_specs=(P("node", None, "local"), P("node", None)),
        check_vma=False,
    )
```

```python
import jax
import jax.numpy as jnp
from jax import lax
from jax.sharding import PartitionSpec as P


def gather_slots(source, source_row, slot_valid):
    padded = jnp.concatenate([source, jnp.zeros((1, source.shape[1]), source.dtype)], axis=0)
    index = jnp.where(slot_valid, source_row, source.shape[0])
    return jnp.take(padded, index, axis=0)


def on_device(grad_out, probs, node_list, weight_down, saved_hidden):
    node_count = lax.axis_size("node")
    tok_rows = node_list.shape[0]
    route_count = node_list.shape[1]
    slot_rows = saved_hidden.shape[1]
    capacity = slot_rows // node_count
    expert_count = weight_down.shape[0]
    node_ids = lax.broadcasted_iota(jnp.int32, (tok_rows, route_count, node_count), 2)
    listed = (node_list[:, :, None] == node_ids).astype(jnp.float32)
    member = jnp.sum((node_list[:, :, None] == node_ids).astype(jnp.int32), axis=1)
    arrival = jnp.cumsum(member, axis=0) - member
    positions = lax.broadcasted_iota(jnp.int32, (tok_rows, node_count, capacity), 2)
    select_mask = (arrival[:, :, None] == positions) & (member[:, :, None] == 1)
    select_count = select_mask.astype(jnp.int32)
    token_iota = lax.broadcasted_iota(jnp.int32, (tok_rows, node_count, capacity), 0)
    source_row = jnp.sum(select_count * token_iota, axis=0)
    slot_valid = jnp.sum(select_count, axis=0) > 0
    select_full = select_mask.astype(jnp.float32)
    grouped = probs.reshape(tok_rows, route_count, expert_count).astype(jnp.float32)
    picked = jnp.einsum("tjm,tjc->tmc", listed, grouped, precision=lax.Precision.HIGHEST)
    prob_send = jnp.einsum(
        "tms,tmc->msc", select_full, picked, precision=lax.Precision.HIGHEST
    ).astype(jnp.bfloat16)
    rows_send = gather_slots(grad_out, source_row, slot_valid)
    width = grad_out.shape[1]
    payload = jnp.concatenate(
        [
            rows_send.reshape(node_count, capacity * width),
            prob_send.reshape(node_count, capacity * expert_count),
        ],
        axis=1,
    )
    payload_in = lax.all_to_all(payload, "node", split_axis=0, concat_axis=0, tiled=True)
    local_count = lax.axis_size("local")
    local_index = lax.axis_index("local")
    pieces = []
    saved_pieces = []
    for step in range(local_count):
        target = (local_index + step) % local_count
        piece = lax.dynamic_slice_in_dim(weight_down, target * width, width, axis=2)
        saved_piece = saved_hidden
        if step:
            pairs = [(j, (j + step) % local_count) for j in range(local_count)]
            piece = lax.ppermute(piece, "local", perm=pairs)
            saved_piece = lax.ppermute(saved_piece, "local", perm=pairs)
        pieces.append(piece)
        saved_pieces.append(saved_piece)
    stacked = jnp.stack(pieces, axis=0)
    block_order = (local_index - jnp.arange(local_count, dtype=jnp.int32)) % local_count
    weight_blocks = jnp.take(stacked, block_order, axis=0)
    score_weights = jnp.einsum(
        "berh,behd->erd",
        jnp.stack(saved_pieces, axis=0),
        stacked,
        preferred_element_type=jnp.float32,
    )
    payload_in, score_weights = lax.optimization_barrier((payload_in, score_weights))
    rows_in = payload_in[:, : capacity * width].reshape(slot_rows, width)
    prob_in = payload_in[:, capacity * width :]
    partial_grads = jnp.einsum(
        "rd,behd->erbh",
        rows_in,
        weight_blocks,
        preferred_element_type=jnp.float32,
    ).reshape(expert_count, slot_rows, -1)
    partial_scores = jnp.sum(rows_in.astype(jnp.float32)[None] * score_weights, axis=2)
    partial_value = jnp.transpose(partial_scores).reshape(node_count, capacity, expert_count)
    summed = jnp.sum(lax.all_gather(partial_value, "local", axis=0, tiled=False), axis=0)
    hidden_grads = lax.psum_scatter(partial_grads, "local", scatter_dimension=2, tiled=True)
    scales = jnp.transpose(prob_in.reshape(slot_rows, expert_count).astype(jnp.float32))
    grad_hidden = (scales[:, :, None] * hidden_grads).astype(jnp.bfloat16)
    returned = lax.all_to_all(summed, "node", split_axis=0, concat_axis=0, tiled=True)
    per_node = jnp.einsum("tms,msc->tmc", select_full, returned, precision=lax.Precision.HIGHEST)
    grad_probs = jnp.einsum("tjm,tmc->tjc", listed, per_node, precision=lax.Precision.HIGHEST)
    return (grad_hidden, grad_probs.reshape(tok_rows, route_count * expert_count))


def solution(mesh):
    return jax.shard_map(
        on_device,
        mesh=mesh,
        in_specs=(
            P("node", "local"),
            P("node", None),
            P("node", None),
            P("node", "local", None),
            P("node", None, "local"),
        ),
        out_specs=(P("node", None, "local"), P("node", None)),
        check_vma=False,
    )
```

```python
import jax
import jax.numpy as jnp
from jax import lax
from jax.sharding import PartitionSpec as P


def gather_slots(source, source_row, slot_valid):
    padded = jnp.concatenate([source, jnp.zeros((1, source.shape[1]), source.dtype)], axis=0)
    index = jnp.where(slot_valid, source_row, source.shape[0])
    return jnp.take(padded, index, axis=0)


def on_device(grad_out, probs, node_list, weight_down, saved_hidden):
    node_count = lax.axis_size("node")
    tok_rows = node_list.shape[0]
    route_count = node_list.shape[1]
    slot_rows = saved_hidden.shape[1]
    capacity = slot_rows // node_count
    expert_count = weight_down.shape[0]
    node_ids = lax.broadcasted_iota(jnp.int32, (tok_rows, route_count, node_count), 2)
    listed = (node_list[:, :, None] == node_ids).astype(jnp.float32)
    member = jnp.sum((node_list[:, :, None] == node_ids).astype(jnp.int32), axis=1)
    arrival = jnp.cumsum(member, axis=0) - member
    positions = lax.broadcasted_iota(jnp.int32, (tok_rows, node_count, capacity), 2)
    select_mask = (arrival[:, :, None] == positions) & (member[:, :, None] == 1)
    select_count = select_mask.astype(jnp.int32)
    token_iota = lax.broadcasted_iota(jnp.int32, (tok_rows, node_count, capacity), 0)
    source_row = jnp.sum(select_count * token_iota, axis=0)
    slot_valid = jnp.sum(select_count, axis=0) > 0
    select_full = select_mask.astype(jnp.float32)
    grouped = probs.reshape(tok_rows, route_count, expert_count).astype(jnp.float32)
    picked = jnp.einsum("tjm,tjc->tmc", listed, grouped, precision=lax.Precision.HIGHEST)
    prob_send = jnp.einsum(
        "tms,tmc->msc", select_full, picked, precision=lax.Precision.HIGHEST
    ).astype(jnp.bfloat16)
    rows_send = gather_slots(grad_out, source_row, slot_valid)
    width = grad_out.shape[1]
    payload = jnp.concatenate(
        [
            rows_send.reshape(node_count, capacity * width),
            prob_send.reshape(node_count, capacity * expert_count),
        ],
        axis=1,
    )
    payload_in = lax.all_to_all(payload, "node", split_axis=0, concat_axis=0, tiled=True)
    rows_in = payload_in[:, : capacity * width].reshape(slot_rows, width)
    prob_in = payload_in[:, capacity * width :]
    local_count = lax.axis_size("local")
    local_index = lax.axis_index("local")
    pieces = []
    for step in range(local_count):
        target = (local_index + step) % local_count
        piece = lax.dynamic_slice_in_dim(weight_down, target * width, width, axis=2)
        if step:
            pairs = [(j, (j + step) % local_count) for j in range(local_count)]
            piece = lax.ppermute(piece, "local", perm=pairs)
        pieces.append(piece)
    stacked = jnp.stack(pieces, axis=0)
    block_order = (local_index - jnp.arange(local_count, dtype=jnp.int32)) % local_count
    weight_blocks = jnp.take(stacked, block_order, axis=0)
    weight_cols = jnp.transpose(weight_blocks, (1, 0, 2, 3)).reshape(expert_count, -1, width)
    partial_grads = jnp.einsum(
        "rd,ehd->erh",
        rows_in,
        weight_cols,
        preferred_element_type=jnp.float32,
    )
    saved_full = lax.all_gather(saved_hidden, "local", axis=2, tiled=True)
    partial_scores = jnp.sum(saved_full.astype(jnp.float32) * partial_grads, axis=2)
    partial_value = jnp.transpose(partial_scores).reshape(node_count, capacity, expert_count)
    summed = jnp.sum(lax.all_gather(partial_value, "local", axis=0, tiled=False), axis=0)
    hidden_grads = lax.psum_scatter(partial_grads, "local", scatter_dimension=2, tiled=True)
    scales = jnp.transpose(prob_in.reshape(slot_rows, expert_count).astype(jnp.float32))
    grad_hidden = (scales[:, :, None] * hidden_grads).astype(jnp.bfloat16)
    returned = lax.all_to_all(summed, "node", split_axis=0, concat_axis=0, tiled=True)
    per_node = jnp.einsum("tms,msc->tmc", select_full, returned, precision=lax.Precision.HIGHEST)
    grad_probs = jnp.einsum("tjm,tmc->tjc", listed, per_node, precision=lax.Precision.HIGHEST)
    return (grad_hidden, grad_probs.reshape(tok_rows, route_count * expert_count))


def solution(mesh):
    return jax.shard_map(
        on_device,
        mesh=mesh,
        in_specs=(
            P("node", "local"),
            P("node", None),
            P("node", None),
            P("node", "local", None),
            P("node", None, "local"),
        ),
        out_specs=(P("node", None, "local"), P("node", None)),
        check_vma=False,
    )
```

```python
import jax
import jax.numpy as jnp
from jax import lax
from jax.sharding import PartitionSpec as P


def gather_slots(source, source_row, slot_valid):
    padded = jnp.concatenate([source, jnp.zeros((1, source.shape[1]), source.dtype)], axis=0)
    index = jnp.where(slot_valid, source_row, source.shape[0])
    return jnp.take(padded, index, axis=0)


def on_device(grad_out, probs, node_list, weight_down, saved_hidden):
    node_count = lax.axis_size("node")
    tok_rows = node_list.shape[0]
    route_count = node_list.shape[1]
    slot_rows = saved_hidden.shape[1]
    capacity = slot_rows // node_count
    expert_count = weight_down.shape[0]
    node_ids = lax.broadcasted_iota(jnp.int32, (tok_rows, route_count, node_count), 2)
    listed = (node_list[:, :, None] == node_ids).astype(jnp.float32)
    member = jnp.sum((node_list[:, :, None] == node_ids).astype(jnp.int32), axis=1)
    arrival = jnp.cumsum(member, axis=0) - member
    positions = lax.broadcasted_iota(jnp.int32, (tok_rows, node_count, capacity), 2)
    select_mask = (arrival[:, :, None] == positions) & (member[:, :, None] == 1)
    select_count = select_mask.astype(jnp.int32)
    token_iota = lax.broadcasted_iota(jnp.int32, (tok_rows, node_count, capacity), 0)
    source_row = jnp.sum(select_count * token_iota, axis=0)
    slot_valid = jnp.sum(select_count, axis=0) > 0
    select_full = select_mask.astype(jnp.float32)
    grouped = probs.reshape(tok_rows, route_count, expert_count).astype(jnp.float32)
    picked = jnp.einsum("tjm,tjc->tmc", listed, grouped, precision=lax.Precision.HIGHEST)
    prob_send = jnp.einsum(
        "tms,tmc->msc", select_full, picked, precision=lax.Precision.HIGHEST
    ).astype(jnp.bfloat16)
    rows_send = jnp.einsum(
        "tms,td->msd",
        select_mask.astype(grad_out.dtype),
        grad_out,
        preferred_element_type=jnp.float32,
    ).astype(grad_out.dtype)
    width = grad_out.shape[1]
    payload = jnp.concatenate(
        [
            rows_send.reshape(node_count, capacity * width),
            prob_send.reshape(node_count, capacity * expert_count),
        ],
        axis=1,
    )
    payload_in = lax.all_to_all(payload, "node", split_axis=0, concat_axis=0, tiled=True)
    rows_in = payload_in[:, : capacity * width].reshape(slot_rows, width)
    prob_in = payload_in[:, capacity * width :]
    local_count = lax.axis_size("local")
    local_index = lax.axis_index("local")
    pieces = []
    for step in range(local_count):
        target = (local_index + step) % local_count
        piece = lax.dynamic_slice_in_dim(weight_down, target * width, width, axis=2)
        if step:
            pairs = [(j, (j + step) % local_count) for j in range(local_count)]
            piece = lax.ppermute(piece, "local", perm=pairs)
        pieces.append(piece)
    stacked = jnp.stack(pieces, axis=0)
    block_order = (local_index - jnp.arange(local_count, dtype=jnp.int32)) % local_count
    weight_blocks = jnp.take(stacked, block_order, axis=0)
    weight_cols = jnp.transpose(weight_blocks, (1, 0, 2, 3)).reshape(expert_count, -1, width)
    partial_grads = jnp.einsum(
        "rd,ehd->erh",
        rows_in,
        weight_cols,
        preferred_element_type=jnp.float32,
    )
    saved_full = lax.all_gather(saved_hidden, "local", axis=2, tiled=True)
    partial_scores = jnp.sum(saved_full.astype(jnp.float32) * partial_grads, axis=2)
    partial_value = jnp.transpose(partial_scores).reshape(node_count, capacity, expert_count)
    summed = jnp.sum(lax.all_gather(partial_value, "local", axis=0, tiled=False), axis=0)
    hidden_grads = lax.psum_scatter(partial_grads, "local", scatter_dimension=2, tiled=True)
    scales = jnp.transpose(prob_in.reshape(slot_rows, expert_count).astype(jnp.float32))
    grad_hidden = (scales[:, :, None] * hidden_grads).astype(jnp.bfloat16)
    returned = lax.all_to_all(summed, "node", split_axis=0, concat_axis=0, tiled=True)
    per_node = jnp.einsum("tms,msc->tmc", select_full, returned, precision=lax.Precision.HIGHEST)
    grad_probs = jnp.einsum("tjm,tmc->tjc", listed, per_node, precision=lax.Precision.HIGHEST)
    return (grad_hidden, grad_probs.reshape(tok_rows, route_count * expert_count))


def solution(mesh):
    return jax.shard_map(
        on_device,
        mesh=mesh,
        in_specs=(
            P("node", "local"),
            P("node", None),
            P("node", None),
            P("node", "local", None),
            P("node", None, "local"),
        ),
        out_specs=(P("node", None, "local"), P("node", None)),
        check_vma=False,
    )
```

```python
import jax
import jax.numpy as jnp
from jax import lax
from jax.sharding import PartitionSpec as P


def gather_slots(source, source_row, slot_valid):
    padded = jnp.concatenate([source, jnp.zeros((1, source.shape[1]), source.dtype)], axis=0)
    index = jnp.where(slot_valid, source_row, source.shape[0])
    return jnp.take(padded, index, axis=0)


def on_device(grad_out, probs, node_list, weight_down, saved_hidden):
    node_count = lax.axis_size("node")
    tok_rows = node_list.shape[0]
    route_count = node_list.shape[1]
    slot_rows = saved_hidden.shape[1]
    capacity = slot_rows // node_count
    expert_count = weight_down.shape[0]
    node_ids = lax.broadcasted_iota(jnp.int32, (tok_rows, route_count, node_count), 2)
    listed = (node_list[:, :, None] == node_ids).astype(jnp.float32)
    member = jnp.sum((node_list[:, :, None] == node_ids).astype(jnp.int32), axis=1)
    arrival = jnp.cumsum(member, axis=0) - member
    positions = lax.broadcasted_iota(jnp.int32, (tok_rows, node_count, capacity), 2)
    select_mask = (arrival[:, :, None] == positions) & (member[:, :, None] == 1)
    select_count = select_mask.astype(jnp.int32)
    token_iota = lax.broadcasted_iota(jnp.int32, (tok_rows, node_count, capacity), 0)
    source_row = jnp.sum(select_count * token_iota, axis=0)
    slot_valid = jnp.sum(select_count, axis=0) > 0
    select_full = select_mask.astype(jnp.float32)
    grouped = probs.reshape(tok_rows, route_count, expert_count).astype(jnp.float32)
    picked = jnp.einsum("tjm,tjc->tmc", listed, grouped, precision=lax.Precision.HIGHEST)
    prob_send = jnp.einsum(
        "tms,tmc->msc", select_full, picked, precision=lax.Precision.HIGHEST
    ).astype(jnp.bfloat16)
    rows_send = jnp.einsum(
        "tms,td->msd",
        select_mask.astype(grad_out.dtype),
        grad_out,
        preferred_element_type=jnp.float32,
    ).astype(grad_out.dtype)
    width = grad_out.shape[1]
    payload = jnp.concatenate(
        [
            rows_send.reshape(node_count, capacity * width),
            prob_send.reshape(node_count, capacity * expert_count),
        ],
        axis=1,
    )
    payload_in = lax.all_to_all(payload, "node", split_axis=0, concat_axis=0, tiled=True)
    rows_in = payload_in[:, : capacity * width].reshape(slot_rows, width)
    prob_in = payload_in[:, capacity * width :]
    local_count = lax.axis_size("local")
    local_index = lax.axis_index("local")
    pieces = []
    for step in range(local_count):
        target = (local_index + step) % local_count
        piece = lax.dynamic_slice_in_dim(weight_down, target * width, width, axis=2)
        if step:
            pairs = [(j, (j + step) % local_count) for j in range(local_count)]
            piece = lax.ppermute(piece, "local", perm=pairs)
        pieces.append(piece)
    stacked = jnp.stack(pieces, axis=0)
    block_order = (local_index - jnp.arange(local_count, dtype=jnp.int32)) % local_count
    weight_blocks = jnp.take(stacked, block_order, axis=0)
    weight_cols = jnp.transpose(weight_blocks, (1, 0, 2, 3)).reshape(expert_count, -1, width)
    saved_full = lax.all_gather(saved_hidden, "local", axis=2, tiled=True)
    score_list = []
    hidden_list = []
    for expert in range(expert_count):
        expert_grads = jnp.einsum(
            "rd,hd->rh",
            rows_in,
            weight_cols[expert],
            preferred_element_type=jnp.float32,
        )
        score_list.append(jnp.sum(saved_full[expert].astype(jnp.float32) * expert_grads, axis=1))
        hidden_list.append(
            lax.psum_scatter(expert_grads, "local", scatter_dimension=1, tiled=True)
        )
    partial_scores = jnp.stack(score_list, axis=0)
    partial_value = jnp.transpose(partial_scores).reshape(node_count, capacity, expert_count)
    summed = jnp.sum(lax.all_gather(partial_value, "local", axis=0, tiled=False), axis=0)
    hidden_grads = jnp.stack(hidden_list, axis=0)
    scales = jnp.transpose(prob_in.reshape(slot_rows, expert_count).astype(jnp.float32))
    grad_hidden = (scales[:, :, None] * hidden_grads).astype(jnp.bfloat16)
    returned = lax.all_to_all(summed, "node", split_axis=0, concat_axis=0, tiled=True)
    per_node = jnp.einsum("tms,msc->tmc", select_full, returned, precision=lax.Precision.HIGHEST)
    grad_probs = jnp.einsum("tjm,tmc->tjc", listed, per_node, precision=lax.Precision.HIGHEST)
    return (grad_hidden, grad_probs.reshape(tok_rows, route_count * expert_count))


def solution(mesh):
    return jax.shard_map(
        on_device,
        mesh=mesh,
        in_specs=(
            P("node", "local"),
            P("node", None),
            P("node", None),
            P("node", "local", None),
            P("node", None, "local"),
        ),
        out_specs=(P("node", None, "local"), P("node", None)),
        check_vma=False,
    )
```

```python
import jax
import jax.numpy as jnp
from jax import lax
from jax.sharding import PartitionSpec as P


def gather_slots(source, source_row, slot_valid):
    padded = jnp.concatenate([source, jnp.zeros((1, source.shape[1]), source.dtype)], axis=0)
    index = jnp.where(slot_valid, source_row, source.shape[0])
    return jnp.take(padded, index, axis=0)


def on_device(grad_out, probs, node_list, weight_down, saved_hidden):
    node_count = lax.axis_size("node")
    tok_rows = node_list.shape[0]
    route_count = node_list.shape[1]
    slot_rows = saved_hidden.shape[1]
    capacity = slot_rows // node_count
    expert_count = weight_down.shape[0]
    node_ids = lax.broadcasted_iota(jnp.int32, (tok_rows, route_count, node_count), 2)
    listed = (node_list[:, :, None] == node_ids).astype(jnp.float32)
    member = jnp.sum((node_list[:, :, None] == node_ids).astype(jnp.int32), axis=1)
    arrival = jnp.cumsum(member, axis=0) - member
    positions = lax.broadcasted_iota(jnp.int32, (tok_rows, node_count, capacity), 2)
    select_mask = (arrival[:, :, None] == positions) & (member[:, :, None] == 1)
    select_count = select_mask.astype(jnp.int32)
    token_iota = lax.broadcasted_iota(jnp.int32, (tok_rows, node_count, capacity), 0)
    source_row = jnp.sum(select_count * token_iota, axis=0)
    slot_valid = jnp.sum(select_count, axis=0) > 0
    select_full = select_mask.astype(jnp.float32)
    grouped = probs.reshape(tok_rows, route_count, expert_count).astype(jnp.float32)
    picked = jnp.einsum("tjm,tjc->tmc", listed, grouped, precision=lax.Precision.HIGHEST)
    prob_send = jnp.einsum(
        "tms,tmc->msc", select_full, picked, precision=lax.Precision.HIGHEST
    ).astype(jnp.bfloat16)
    rows_send = jnp.einsum(
        "tms,td->msd",
        select_mask.astype(grad_out.dtype),
        grad_out,
        preferred_element_type=jnp.float32,
    ).astype(grad_out.dtype)
    width = grad_out.shape[1]
    payload = jnp.concatenate(
        [
            rows_send.reshape(node_count, capacity * width),
            prob_send.reshape(node_count, capacity * expert_count),
        ],
        axis=1,
    )
    payload_in = lax.all_to_all(payload, "node", split_axis=0, concat_axis=0, tiled=True)
    rows_in = payload_in[:, : capacity * width].reshape(slot_rows, width)
    prob_in = payload_in[:, capacity * width :]
    local_count = lax.axis_size("local")
    local_index = lax.axis_index("local")
    pieces = []
    for step in range(local_count):
        target = (local_index + step) % local_count
        piece = lax.dynamic_slice_in_dim(weight_down, target * width, width, axis=2)
        if step:
            pairs = [(j, (j + step) % local_count) for j in range(local_count)]
            piece = lax.ppermute(piece, "local", perm=pairs)
        pieces.append(piece)
    stacked = jnp.stack(pieces, axis=0)
    block_order = (local_index - jnp.arange(local_count, dtype=jnp.int32)) % local_count
    weight_blocks = jnp.take(stacked, block_order, axis=0)
    weight_cols = jnp.transpose(weight_blocks, (1, 0, 2, 3)).reshape(expert_count, -1, width)
    partial_grads = jnp.einsum(
        "rd,ehd->erh",
        rows_in,
        weight_cols,
        preferred_element_type=jnp.float32,
    )
    saved_full = lax.all_gather(saved_hidden, "local", axis=2, tiled=True)
    held_grads = lax.optimization_barrier(partial_grads)
    partial_scores = jnp.sum(saved_full.astype(jnp.float32) * held_grads, axis=2)
    partial_value = jnp.transpose(partial_scores).reshape(node_count, capacity, expert_count)
    summed = jnp.sum(lax.all_gather(partial_value, "local", axis=0, tiled=False), axis=0)
    hidden_grads = lax.psum_scatter(partial_grads, "local", scatter_dimension=2, tiled=True)
    scales = jnp.transpose(prob_in.reshape(slot_rows, expert_count).astype(jnp.float32))
    grad_hidden = (scales[:, :, None] * hidden_grads).astype(jnp.bfloat16)
    returned = lax.all_to_all(summed, "node", split_axis=0, concat_axis=0, tiled=True)
    per_node = jnp.einsum("tms,msc->tmc", select_full, returned, precision=lax.Precision.HIGHEST)
    grad_probs = jnp.einsum("tjm,tmc->tjc", listed, per_node, precision=lax.Precision.HIGHEST)
    return (grad_hidden, grad_probs.reshape(tok_rows, route_count * expert_count))


def solution(mesh):
    return jax.shard_map(
        on_device,
        mesh=mesh,
        in_specs=(
            P("node", "local"),
            P("node", None),
            P("node", None),
            P("node", "local", None),
            P("node", None, "local"),
        ),
        out_specs=(P("node", None, "local"), P("node", None)),
        check_vma=False,
    )
```

```python
import jax
import jax.numpy as jnp
from jax import lax
from jax.sharding import PartitionSpec as P


def gather_slots(source, source_row, slot_valid):
    padded = jnp.concatenate([source, jnp.zeros((1, source.shape[1]), source.dtype)], axis=0)
    index = jnp.where(slot_valid, source_row, source.shape[0])
    return jnp.take(padded, index, axis=0)


def on_device(grad_out, probs, node_list, weight_down, saved_hidden):
    node_count = lax.axis_size("node")
    tok_rows = node_list.shape[0]
    route_count = node_list.shape[1]
    slot_rows = saved_hidden.shape[1]
    capacity = slot_rows // node_count
    expert_count = weight_down.shape[0]
    node_ids = lax.broadcasted_iota(jnp.int32, (tok_rows, route_count, node_count), 2)
    listed = (node_list[:, :, None] == node_ids).astype(jnp.float32)
    member = jnp.sum((node_list[:, :, None] == node_ids).astype(jnp.int32), axis=1)
    arrival = jnp.cumsum(member, axis=0) - member
    positions = lax.broadcasted_iota(jnp.int32, (tok_rows, node_count, capacity), 2)
    select_mask = (arrival[:, :, None] == positions) & (member[:, :, None] == 1)
    select_count = select_mask.astype(jnp.int32)
    token_iota = lax.broadcasted_iota(jnp.int32, (tok_rows, node_count, capacity), 0)
    source_row = jnp.sum(select_count * token_iota, axis=0)
    slot_valid = jnp.sum(select_count, axis=0) > 0
    select_full = select_mask.astype(jnp.float32)
    grouped = probs.reshape(tok_rows, route_count, expert_count).astype(jnp.float32)
    picked = jnp.einsum("tjm,tjc->tmc", listed, grouped, precision=lax.Precision.HIGHEST)
    prob_send = jnp.einsum(
        "tms,tmc->msc", select_full, picked, precision=lax.Precision.HIGHEST
    ).astype(jnp.bfloat16)
    rows_send = jnp.einsum(
        "tms,td->msd",
        select_mask.astype(grad_out.dtype),
        grad_out,
        preferred_element_type=jnp.float32,
    ).astype(grad_out.dtype)
    width = grad_out.shape[1]
    halves = 2
    per_half = capacity // halves
    payload = jnp.concatenate(
        [
            rows_send.reshape(node_count, halves, per_half * width),
            prob_send.reshape(node_count, halves, per_half * expert_count),
        ],
        axis=2,
    )
    payload_in = lax.all_to_all(payload, "node", split_axis=0, concat_axis=0, tiled=True)
    rows_in = payload_in[:, :, : per_half * width].reshape(slot_rows, width)
    prob_in = payload_in[:, :, per_half * width :]
    local_count = lax.axis_size("local")
    local_index = lax.axis_index("local")
    pieces = []
    for step in range(local_count):
        target = (local_index + step) % local_count
        piece = lax.dynamic_slice_in_dim(weight_down, target * width, width, axis=2)
        if step:
            pairs = [(j, (j + step) % local_count) for j in range(local_count)]
            piece = lax.ppermute(piece, "local", perm=pairs)
        pieces.append(piece)
    stacked = jnp.stack(pieces, axis=0)
    block_order = (local_index - jnp.arange(local_count, dtype=jnp.int32)) % local_count
    weight_blocks = jnp.take(stacked, block_order, axis=0)
    weight_cols = jnp.transpose(weight_blocks, (1, 0, 2, 3)).reshape(expert_count, -1, width)
    partial_grads = jnp.einsum(
        "rd,ehd->erh",
        rows_in,
        weight_cols,
        preferred_element_type=jnp.float32,
    )
    saved_full = lax.all_gather(saved_hidden, "local", axis=2, tiled=True)
    partial_scores = jnp.sum(saved_full.astype(jnp.float32) * partial_grads, axis=2)
    partial_value = jnp.transpose(partial_scores).reshape(node_count, capacity, expert_count)
    summed = jnp.sum(lax.all_gather(partial_value, "local", axis=0, tiled=False), axis=0)
    hidden_grads = lax.psum_scatter(partial_grads, "local", scatter_dimension=2, tiled=True)
    scales = jnp.transpose(prob_in.reshape(slot_rows, expert_count).astype(jnp.float32))
    grad_hidden = (scales[:, :, None] * hidden_grads).astype(jnp.bfloat16)
    returned = lax.all_to_all(summed, "node", split_axis=0, concat_axis=0, tiled=True)
    per_node = jnp.einsum("tms,msc->tmc", select_full, returned, precision=lax.Precision.HIGHEST)
    grad_probs = jnp.einsum("tjm,tmc->tjc", listed, per_node, precision=lax.Precision.HIGHEST)
    return (grad_hidden, grad_probs.reshape(tok_rows, route_count * expert_count))


def solution(mesh):
    return jax.shard_map(
        on_device,
        mesh=mesh,
        in_specs=(
            P("node", "local"),
            P("node", None),
            P("node", None),
            P("node", "local", None),
            P("node", None, "local"),
        ),
        out_specs=(P("node", None, "local"), P("node", None)),
        check_vma=False,
    )
```

```python
import jax
import jax.numpy as jnp
from jax import lax
from jax.sharding import PartitionSpec as P


def gather_slots(source, source_row, slot_valid):
    padded = jnp.concatenate([source, jnp.zeros((1, source.shape[1]), source.dtype)], axis=0)
    index = jnp.where(slot_valid, source_row, source.shape[0])
    return jnp.take(padded, index, axis=0)


def on_device(grad_out, probs, node_list, weight_down, saved_hidden):
    node_count = lax.axis_size("node")
    tok_rows = node_list.shape[0]
    route_count = node_list.shape[1]
    slot_rows = saved_hidden.shape[1]
    capacity = slot_rows // node_count
    expert_count = weight_down.shape[0]
    node_ids = lax.broadcasted_iota(jnp.int32, (tok_rows, route_count, node_count), 2)
    listed = (node_list[:, :, None] == node_ids).astype(jnp.float32)
    member = jnp.sum((node_list[:, :, None] == node_ids).astype(jnp.int32), axis=1)
    arrival = jnp.cumsum(member, axis=0) - member
    positions = lax.broadcasted_iota(jnp.int32, (tok_rows, node_count, capacity), 2)
    select_mask = (arrival[:, :, None] == positions) & (member[:, :, None] == 1)
    select_count = select_mask.astype(jnp.int32)
    token_iota = lax.broadcasted_iota(jnp.int32, (tok_rows, node_count, capacity), 0)
    source_row = jnp.sum(select_count * token_iota, axis=0)
    slot_valid = jnp.sum(select_count, axis=0) > 0
    select_full = select_mask.astype(jnp.float32)
    grouped = probs.reshape(tok_rows, route_count, expert_count).astype(jnp.float32)
    picked = jnp.einsum("tjm,tjc->tmc", listed, grouped, precision=lax.Precision.HIGHEST)
    prob_send = jnp.einsum(
        "tms,tmc->msc", select_full, picked, precision=lax.Precision.HIGHEST
    ).astype(jnp.bfloat16)
    rows_send = jnp.einsum(
        "tms,td->msd",
        select_mask.astype(grad_out.dtype),
        grad_out,
        preferred_element_type=jnp.float32,
    ).astype(grad_out.dtype)
    width = grad_out.shape[1]
    halves = 2
    per_half = capacity // halves
    payload = jnp.concatenate(
        [
            rows_send.reshape(node_count, halves, per_half * width),
            prob_send.reshape(node_count, halves, per_half * expert_count),
        ],
        axis=2,
    )
    payload_in = lax.all_to_all(payload, "node", split_axis=0, concat_axis=0, tiled=True)
    rows_in = payload_in[:, :, : per_half * width].reshape(slot_rows, width)
    prob_in = payload_in[:, :, per_half * width :]
    local_count = lax.axis_size("local")
    local_index = lax.axis_index("local")
    hidden_local = weight_down.shape[1]
    weight_buffer = jnp.zeros((expert_count, local_count, hidden_local, width), weight_down.dtype)
    for step in range(local_count):
        target = (local_index + step) % local_count
        piece = lax.dynamic_slice_in_dim(weight_down, target * width, width, axis=2)
        if step:
            pairs = [(j, (j + step) % local_count) for j in range(local_count)]
            piece = lax.ppermute(piece, "local", perm=pairs)
        block = (local_index - step) % local_count
        weight_buffer = lax.dynamic_update_slice(weight_buffer, piece[:, None], (0, block, 0, 0))
    weight_cols = weight_buffer.reshape(expert_count, -1, width)
    partial_grads = jnp.einsum(
        "rd,ehd->erh",
        rows_in,
        weight_cols,
        preferred_element_type=jnp.float32,
    )
    saved_full = lax.all_gather(saved_hidden, "local", axis=2, tiled=True)
    partial_scores = jnp.sum(saved_full.astype(jnp.float32) * partial_grads, axis=2)
    partial_value = jnp.transpose(partial_scores).reshape(node_count, capacity, expert_count)
    summed = jnp.sum(lax.all_gather(partial_value, "local", axis=0, tiled=False), axis=0)
    hidden_grads = lax.psum_scatter(partial_grads, "local", scatter_dimension=2, tiled=True)
    scales = jnp.transpose(prob_in.reshape(slot_rows, expert_count).astype(jnp.float32))
    grad_hidden = (scales[:, :, None] * hidden_grads).astype(jnp.bfloat16)
    returned = lax.all_to_all(summed, "node", split_axis=0, concat_axis=0, tiled=True)
    per_node = jnp.einsum("tms,msc->tmc", select_full, returned, precision=lax.Precision.HIGHEST)
    grad_probs = jnp.einsum("tjm,tmc->tjc", listed, per_node, precision=lax.Precision.HIGHEST)
    return (grad_hidden, grad_probs.reshape(tok_rows, route_count * expert_count))


def solution(mesh):
    return jax.shard_map(
        on_device,
        mesh=mesh,
        in_specs=(
            P("node", "local"),
            P("node", None),
            P("node", None),
            P("node", "local", None),
            P("node", None, "local"),
        ),
        out_specs=(P("node", None, "local"), P("node", None)),
        check_vma=False,
    )
```

```python
import jax
import jax.numpy as jnp
from jax import lax
from jax.sharding import PartitionSpec as P


def gather_slots(source, source_row, slot_valid):
    padded = jnp.concatenate([source, jnp.zeros((1, source.shape[1]), source.dtype)], axis=0)
    index = jnp.where(slot_valid, source_row, source.shape[0])
    return jnp.take(padded, index, axis=0)


def on_device(grad_out, probs, node_list, weight_down, saved_hidden):
    node_count = lax.axis_size("node")
    tok_rows = node_list.shape[0]
    route_count = node_list.shape[1]
    slot_rows = saved_hidden.shape[1]
    capacity = slot_rows // node_count
    expert_count = weight_down.shape[0]
    node_ids = lax.broadcasted_iota(jnp.int32, (tok_rows, route_count, node_count), 2)
    listed = (node_list[:, :, None] == node_ids).astype(jnp.float32)
    member = jnp.sum((node_list[:, :, None] == node_ids).astype(jnp.int32), axis=1)
    arrival = jnp.cumsum(member, axis=0) - member
    positions = lax.broadcasted_iota(jnp.int32, (tok_rows, node_count, capacity), 2)
    select_mask = (arrival[:, :, None] == positions) & (member[:, :, None] == 1)
    select_count = select_mask.astype(jnp.int32)
    token_iota = lax.broadcasted_iota(jnp.int32, (tok_rows, node_count, capacity), 0)
    source_row = jnp.sum(select_count * token_iota, axis=0)
    slot_valid = jnp.sum(select_count, axis=0) > 0
    select_full = select_mask.astype(jnp.float32)
    grouped = probs.reshape(tok_rows, route_count, expert_count).astype(jnp.float32)
    picked = jnp.einsum("tjm,tjc->tmc", listed, grouped, precision=lax.Precision.HIGHEST)
    prob_send = jnp.einsum(
        "tms,tmc->msc", select_full, picked, precision=lax.Precision.HIGHEST
    ).astype(jnp.bfloat16)
    rows_send = jnp.einsum(
        "tms,td->msd",
        select_mask.astype(grad_out.dtype),
        grad_out,
        preferred_element_type=jnp.float32,
    ).astype(grad_out.dtype)
    width = grad_out.shape[1]
    halves = 2
    per_half = capacity // halves
    payload = jnp.concatenate(
        [
            rows_send.reshape(node_count, halves, per_half * width),
            prob_send.reshape(node_count, halves, per_half * expert_count),
        ],
        axis=2,
    )
    payload_in = lax.all_to_all(payload, "node", split_axis=0, concat_axis=0, tiled=True)
    rows_in = payload_in[:, :, : per_half * width].reshape(slot_rows, width)
    prob_in = payload_in[:, :, per_half * width :]
    local_count = lax.axis_size("local")
    local_index = lax.axis_index("local")
    hidden_local = weight_down.shape[1]
    weight_buffer = jnp.zeros((expert_count, local_count, hidden_local, width), weight_down.dtype)
    for step in range(local_count):
        target = (local_index + step) % local_count
        piece = lax.dynamic_slice_in_dim(weight_down, target * width, width, axis=2)
        if step:
            pairs = [(j, (j + step) % local_count) for j in range(local_count)]
            piece = lax.ppermute(piece, "local", perm=pairs)
            if step == 1:
                piece, saved_late = lax.optimization_barrier((piece, saved_hidden))
        block = (local_index - step) % local_count
        weight_buffer = lax.dynamic_update_slice(weight_buffer, piece[:, None], (0, block, 0, 0))
    weight_cols = weight_buffer.reshape(expert_count, -1, width)
    partial_grads = jnp.einsum(
        "rd,ehd->erh",
        rows_in,
        weight_cols,
        preferred_element_type=jnp.float32,
    )
    saved_full = lax.all_gather(saved_late, "local", axis=2, tiled=True)
    partial_scores = jnp.sum(saved_full.astype(jnp.float32) * partial_grads, axis=2)
    partial_value = jnp.transpose(partial_scores).reshape(node_count, capacity, expert_count)
    summed = jnp.sum(lax.all_gather(partial_value, "local", axis=0, tiled=False), axis=0)
    hidden_grads = lax.psum_scatter(partial_grads, "local", scatter_dimension=2, tiled=True)
    scales = jnp.transpose(prob_in.reshape(slot_rows, expert_count).astype(jnp.float32))
    grad_hidden = (scales[:, :, None] * hidden_grads).astype(jnp.bfloat16)
    returned = lax.all_to_all(summed, "node", split_axis=0, concat_axis=0, tiled=True)
    per_node = jnp.einsum("tms,msc->tmc", select_full, returned, precision=lax.Precision.HIGHEST)
    grad_probs = jnp.einsum("tjm,tmc->tjc", listed, per_node, precision=lax.Precision.HIGHEST)
    return (grad_hidden, grad_probs.reshape(tok_rows, route_count * expert_count))


def solution(mesh):
    return jax.shard_map(
        on_device,
        mesh=mesh,
        in_specs=(
            P("node", "local"),
            P("node", None),
            P("node", None),
            P("node", "local", None),
            P("node", None, "local"),
        ),
        out_specs=(P("node", None, "local"), P("node", None)),
        check_vma=False,
    )
```
